256 devices in a mesh: row: 16 (over x_hi, z), col: 16 (over x_lo, y, core).
Axes of the slice: x: 4 (x_hi: 2, x_lo: 2; x = x_hi * 2 + x_lo), y: 4, z: 8, core: 2. Of those that a mesh axis runs over, the one named last changes fastest.
Arguments:
- features: bfloat16 [3, 256, 256, 1024], P(None, 'row', 'col'), may hold values from -6 to 6
- dw_kernel: bfloat16 [7, 7, 1024], replicated, may hold values from -0.875 to 0.875
- ln_gain: float32 [1024], replicated, may hold values from 0.1 to 1.9
- w_in: bfloat16 [1024, 4096], P(None, 'col'), may hold values from -0.1875 to 0.1875
- w_down: bfloat16 [1024, 4096], P(None, 'col'), may hold values from -0.09375 to 0.09375
- gamma: float32 [1024], replicated, may hold values from 0.3 to 1.5
- labels: int32 [3, 256, 256], P(None, 'row', 'col'), may hold values from 0 to 15
- valid: int32 [3, 256, 256], P(None, 'row', 'col'), may hold values 0 or 1
Outputs:
- gram: float32 [1024, 1024], P(('row', 'col'))
- cross: float32 [1024, 16], P(('row', 'col'))
The draws below stay inside these ranges and needn't reach their ends.
All inputs are finite; a program needn't handle non-finite values. No bound on the sum of `valid` on one device may be relied on, other than what follows from the above.
Results may differ from the reference program's by a relative error of at most 0.0037.
Values may be sent and summed in bfloat16 or wider, within the bound.
No kernel may reach another device: no remote copies, remote signals or barrier semaphores. Data moves between devices by JAX's collectives and lax.ppermute only.
A program may use at most 128 MiB of HBM per device.

```python
import math
import jax
import jax.numpy as jnp
from jax import lax

D = 1024
HID = 4096
NCLS = 16
KSIZE = 7
TILES = 3
NH = 256
NW = 256
TOTAL = 196608


def plant(drawn, rng, least, top_value):
    place = [jax.random.randint(jax.random.fold_in(rng, axis), (), 0, length) for axis, length in enumerate(drawn.shape)]
    widest = drawn.shape.index(max(drawn.shape))
    next_to = place[:widest] + [(place[widest] + 1) % drawn.shape[widest]] + place[widest + 1:]
    return drawn.at[tuple(place)].set(least).at[tuple(next_to)].set(top_value)


def raised(drawn, key, source, target, shards_of, factor):
    def block_of(dim):
        return (jnp.arange(drawn.shape[dim]) // (drawn.shape[dim] // shards_of)).reshape((-1,) + (1,) * (drawn.ndim - 1 - dim))

    first = jax.random.permutation(key, shards_of)[block_of(target)]
    far = (block_of(target) + shards_of // 2) % shards_of
    return jnp.where((block_of(source) == first) | (block_of(source) == far), factor * drawn, drawn)


def levels(stream_key, shape, pieces, low, top_value):
    factor_of = 1.0
    for position, parts in pieces:
        draws = jax.random.uniform(jax.random.fold_in(jax.random.fold_in(stream_key, 6), position), (parts,), jnp.float32, low / len(pieces), top_value / len(pieces))
        factor_of = factor_of * jnp.repeat(jnp.exp(draws), shape[position] // parts).reshape((-1,) + (1,) * (len(shape) - 1 - position))
    return factor_of


def noise(own_key, dims, scale, limit, shards=(), kind=jnp.bfloat16):
    values = scale * jax.random.normal(own_key, dims, jnp.float32)
    if shards:
        values = values * levels(own_key, dims, shards, -0.22, 0.18)
    return jnp.clip(values, -limit, limit).astype(kind)


def gaussian_with(stream_key, extent, deviation, bound, pieces, heavy, kind=jnp.bfloat16):
    drawn = deviation * jax.random.normal(stream_key, extent, jnp.float32)
    if pieces:
        drawn = drawn * levels(stream_key, extent, pieces, -0.22, 0.18)
    return jnp.clip(raised(drawn, jax.random.fold_in(stream_key, 3), *heavy), -bound, bound).astype(kind)


def setup_inputs(seed: int = 0) -> dict:
    arg_keys = jax.random.split(jax.random.key(seed), 9)
    return {
        "features": gaussian_with(arg_keys[0], (TILES, NH, NW, D), 1.0, 6.0, ((1, 16), (2, 16)), (1, 3, 16, 2.0)),
        "dw_kernel": noise(arg_keys[1], (KSIZE, KSIZE, D), (KSIZE * KSIZE) ** -0.5, 0.875),
        "ln_gain": jnp.clip(1.0 + 0.18 * jax.random.normal(arg_keys[2], (D,), jnp.float32), 0.1, 1.9),
        "w_in": noise(arg_keys[3], (D, HID), D ** -0.5, 0.1875, ((1, 16),)),
        "w_down": noise(arg_keys[4], (D, HID), HID ** -0.5, 0.09375, ((1, 16),)),
        "gamma": jnp.clip(jnp.exp(jax.random.uniform(arg_keys[5], (D,), jnp.float32, math.log(0.3), math.log(1.5))), 0.3, 1.5),
        "labels": plant(jax.random.randint(arg_keys[6], (TILES, NH, NW), 0, NCLS), jax.random.fold_in(arg_keys[6], 1), 0, NCLS - 1).astype(jnp.int32),
        "valid": plant((jax.random.randint(arg_keys[7], (TILES, NH, NW), 0, 8) < 7).astype(jnp.int32), jax.random.fold_in(arg_keys[7], 1), 0, 1),
    }


def block_stats(carry, inputs, dw_kernel, ln_gain, w_in, w_down, gamma):
    scene, lab, msk = inputs
    high, wide, width = scene.shape
    padded = jnp.pad(scene.astype(jnp.float32), ((3, 3), (3, 3), (0, 0)))
    kernel = dw_kernel.astype(jnp.float32)
    conv = jnp.zeros((high, wide, width), jnp.float32)
    for i in range(KSIZE):
        for j in range(KSIZE):
            conv = conv + padded[i:i + high, j:j + wide, :] * kernel[i, j]
    count = high * wide
    rows = conv.reshape(count, width)
    mean = lax.optimization_barrier(jnp.mean(rows, axis=-1, keepdims=True))
    centered = rows - mean
    var = lax.optimization_barrier(jnp.mean(centered * centered, axis=-1, keepdims=True))
    normed = (centered * lax.rsqrt(var + 1e-06) * ln_gain).astype(jnp.bfloat16)
    hidden = jax.nn.gelu(jnp.dot(normed, w_in, preferred_element_type=jnp.float32), approximate=False).astype(jnp.bfloat16)
    branch = jnp.dot(hidden, w_down.T, preferred_element_type=jnp.float32)
    out = (scene.reshape(count, width).astype(jnp.float32) + gamma * branch).astype(jnp.bfloat16)
    keep = msk.reshape(count, 1)
    masked = out * keep.astype(jnp.bfloat16)
    classes = jnp.arange(NCLS, dtype=jnp.int32)
    onehot = (lab.reshape(count, 1) == classes[None, :]).astype(jnp.float32)
    targets = ((onehot - 1.0 / NCLS) * keep.astype(jnp.float32)).astype(jnp.bfloat16)
    gram_part = lax.dot_general(masked, out, (((0,), (0,)), ((), ())), preferred_element_type=jnp.float32)
    cross_part = lax.dot_general(out, targets, (((0,), (0,)), ((), ())), preferred_element_type=jnp.float32)
    return ((carry[0] + gram_part, carry[1] + cross_part), None)

def reference(features, dw_kernel, ln_gain, w_in, w_down, gamma, labels, valid):
    width = features.shape[3]
    init = (jnp.zeros((width, width), jnp.float32), jnp.zeros((width, NCLS), jnp.float32))

    def step(carry, inputs):
        return block_stats(carry, inputs, dw_kernel, ln_gain, w_in, w_down, gamma)
    (gram_sum, cross_sum), unused = lax.scan(step, init, (features, labels, valid))
    total = float(TOTAL)
    return (gram_sum / total, cross_sum / jnp.sqrt(jnp.float32(total)))
```

```python
import jax
import jax.numpy as jnp
from jax import lax
from jax.sharding import PartitionSpec as P

NCLS = 16
KSIZE = 7


def with_halo(shard, sides, width):
    for axis, dim in sides:
        size, length = (lax.axis_size(axis), shard.shape[dim])
        up = [(i, (i + 1) % size) for i in range(size - 1)]
        down = [(j, i) for i, j in up]
        last = lax.slice_in_dim(shard, length - width, length, axis=dim)
        leading = lax.slice_in_dim(shard, 0, width, axis=dim)
        before = lax.ppermute(last, axis, up)
        after = lax.ppermute(leading, axis, down)
        shard = jnp.concatenate([before, shard, after], axis=dim)
    return shard


def apply_norm(rows, ln_gain):
    mean = jnp.mean(rows, axis=-1, keepdims=True)
    centered = rows - mean
    var = jnp.mean(centered * centered, axis=-1, keepdims=True)
    return (centered * lax.rsqrt(var + 1e-06) * ln_gain).astype(jnp.bfloat16)


def expand(normed, piece):
    return jax.nn.gelu(
        jnp.dot(normed, piece, preferred_element_type=jnp.float32), approximate=False
    ).astype(jnp.bfloat16)


def contract(hidden, piece):
    return lax.dot_general(
        hidden, piece, (((1,), (1,)), ((), ())), preferred_element_type=jnp.float32
    )


def col_first(rows):
    count, width = rows.shape
    nrow, ncol = lax.axis_size("row"), lax.axis_size("col")
    split = rows.reshape(count, nrow, ncol, width // (nrow * ncol))
    return split.transpose(0, 2, 1, 3).reshape(count, width)


def on_device(features, dw_kernel, ln_gain, w_in, w_down, gamma, labels, valid):
    tiles, high, wide, width = features.shape
    padded = with_halo(features, (("row", 1), ("col", 2)), 3).astype(jnp.float32)
    kernel = dw_kernel.astype(jnp.float32)
    conv = jnp.zeros((tiles, high, wide, width), jnp.float32)
    for i in range(KSIZE):
        for j in range(KSIZE):
            conv = conv + padded[:, i : i + high, j : j + wide, :] * kernel[i, j]
    count = tiles * high * wide
    normed = apply_norm(conv.reshape(count, width), ln_gain)
    hidden = expand(normed, lax.all_gather(w_in, "col", axis=1, tiled=True))
    branch = contract(hidden, lax.all_gather(w_down, "col", axis=1, tiled=True))
    out = (features.reshape(count, width).astype(jnp.float32) + gamma * branch).astype(jnp.bfloat16)
    keep = valid.reshape(count, 1)
    masked = out * keep.astype(jnp.bfloat16)
    classes = jnp.arange(NCLS, dtype=jnp.int32)
    onehot = (labels.reshape(count, 1) == classes[None, :]).astype(jnp.float32)
    targets = ((onehot - 1.0 / NCLS) * keep.astype(jnp.float32)).astype(jnp.bfloat16)
    gram_part = lax.dot_general(
        col_first(masked), out, (((0,), (0,)), ((), ())), preferred_element_type=jnp.float32
    )
    cross_part = lax.dot_general(
        col_first(out), targets, (((0,), (0,)), ((), ())), preferred_element_type=jnp.float32
    )
    parts = lax.psum_scatter((gram_part, cross_part), "col", scatter_dimension=0, tiled=True)
    gram_sum, cross_sum = lax.psum_scatter(parts, "row", scatter_dimension=0, tiled=True)
    total = float(tiles * high * lax.axis_size("row") * wide * lax.axis_size("col"))
    return (gram_sum / total, cross_sum / jnp.sqrt(jnp.float32(total)))


def solution(mesh):
    return jax.shard_map(
        on_device,
        mesh=mesh,
        in_specs=(
            P(None, "row", "col", None),
            P(),
            P(),
            P(None, "col"),
            P(None, "col"),
            P(),
            P(None, "row", "col"),
            P(None, "row", "col"),
        ),
        out_specs=(P(("row", "col"), None), P(("row", "col"), None)),
        check_vma=False,
    )
```

```python
import jax
import jax.numpy as jnp
from jax import lax
from jax.sharding import PartitionSpec as P

NCLS = 16
KSIZE = 7


def with_halo(shard, sides, width):
    for axis, dim in sides:
        size, length = (lax.axis_size(axis), shard.shape[dim])
        up = [(i, (i + 1) % size) for i in range(size - 1)]
        down = [(j, i) for i, j in up]
        last = lax.slice_in_dim(shard, length - width, length, axis=dim)
        leading = lax.slice_in_dim(shard, 0, width, axis=dim)
        before = lax.ppermute(last, axis, up)
        after = lax.ppermute(leading, axis, down)
        shard = jnp.concatenate([before, shard, after], axis=dim)
    return shard


def apply_norm(rows, ln_gain):
    mean = jnp.mean(rows, axis=-1, keepdims=True)
    centered = rows - mean
    var = jnp.mean(centered * centered, axis=-1, keepdims=True)
    return (centered * lax.rsqrt(var + 1e-06) * ln_gain).astype(jnp.bfloat16)


def expand(normed, piece):
    return jax.nn.gelu(
        jnp.dot(normed, piece, preferred_element_type=jnp.float32), approximate=False
    ).astype(jnp.bfloat16)


def contract(hidden, piece):
    return lax.dot_general(
        hidden, piece, (((1,), (1,)), ((), ())), preferred_element_type=jnp.float32
    )


HALVING_BITS = (0, 1, 3, 4, 2, 5, 7, 6)


def halving_order(rows):
    count, width = rows.shape
    nbits = len(HALVING_BITS)
    split = rows.reshape((count,) + (2,) * nbits + (width >> nbits,))
    order = (0,) + tuple(nbits - bit for bit in HALVING_BITS) + (nbits + 1,)
    return split.transpose(order).reshape(count, width)


def halving_sum(part, axes):
    size = 1
    for axis in axes:
        size *= lax.axis_size(axis)
    me = lax.axis_index(axes)
    for bit in HALVING_BITS:
        mine = (me >> bit) & 1
        halves = part.reshape((2, part.shape[0] // 2) + part.shape[1:])
        keep = lax.dynamic_index_in_dim(halves, mine, 0, keepdims=False)
        send = lax.dynamic_index_in_dim(halves, 1 - mine, 0, keepdims=False)
        pairs = [(i, i ^ (1 << bit)) for i in range(size)]
        part = keep + lax.ppermute(send, axes, pairs)
    return part


def targets_of(labels, count):
    classes = jnp.arange(NCLS, dtype=jnp.int32)
    onehot = (labels.reshape(count, 1) == classes[None, :]).astype(jnp.float32)
    return (onehot - 1.0 / NCLS).astype(jnp.bfloat16)


def on_device(features, dw_kernel, ln_gain, w_in, w_down, gamma, labels, valid):
    tiles, high, wide, width = features.shape
    padded = with_halo(features, (("row", 1), ("col", 2)), 3).astype(jnp.float32)
    kernel = dw_kernel.astype(jnp.float32)
    conv = jnp.zeros((tiles, high, wide, width), jnp.float32)
    for i in range(KSIZE):
        for j in range(KSIZE):
            conv = conv + padded[:, i : i + high, j : j + wide, :] * kernel[i, j]
    count = tiles * high * wide
    normed = apply_norm(conv.reshape(count, width), ln_gain)
    hidden = expand(normed, lax.all_gather(w_in, "col", axis=1, tiled=True))
    branch = contract(hidden, lax.all_gather(w_down, "col", axis=1, tiled=True))
    out = (features.reshape(count, width).astype(jnp.float32) + gamma * branch).astype(jnp.bfloat16)
    keep = valid.reshape(count, 1)
    masked = out * keep.astype(jnp.bfloat16)
    both = lax.dot_general(
        halving_order(masked),
        jnp.concatenate([out, targets_of(labels, count)], axis=1),
        (((0,), (0,)), ((), ())),
        preferred_element_type=jnp.float32,
    )
    summed = halving_sum(both, ("row", "col"))
    gram_sum, cross_sum = summed[:, :width], summed[:, width:]
    total = float(tiles * high * lax.axis_size("row") * wide * lax.axis_size("col"))
    return (gram_sum / total, cross_sum / jnp.sqrt(jnp.float32(total)))


def solution(mesh):
    return jax.shard_map(
        on_device,
        mesh=mesh,
        in_specs=(
            P(None, "row", "col", None),
            P(),
            P(),
            P(None, "col"),
            P(None, "col"),
            P(),
            P(None, "row", "col"),
            P(None, "row", "col"),
        ),
        out_specs=(P(("row", "col"), None), P(("row", "col"), None)),
        check_vma=False,
    )
```

```python
import jax
import jax.numpy as jnp
from jax import lax
from jax.sharding import PartitionSpec as P

NCLS = 16
KSIZE = 7
LANES = 128


def with_halo(shard, sides, width):
    for axis, dim in sides:
        size, length = (lax.axis_size(axis), shard.shape[dim])
        up = [(i, (i + 1) % size) for i in range(size - 1)]
        down = [(j, i) for i, j in up]
        last = lax.slice_in_dim(shard, length - width, length, axis=dim)
        leading = lax.slice_in_dim(shard, 0, width, axis=dim)
        before = lax.ppermute(last, axis, up)
        after = lax.ppermute(leading, axis, down)
        shard = jnp.concatenate([before, shard, after], axis=dim)
    return shard


def apply_norm(rows, ln_gain):
    mean = jnp.mean(rows, axis=(-2, -1), keepdims=True)
    centered = rows - mean
    var = jnp.mean(centered * centered, axis=(-2, -1), keepdims=True)
    return (centered * lax.rsqrt(var + 1e-06) * ln_gain).astype(jnp.bfloat16)


def expand(normed, piece):
    return jax.nn.gelu(
        jnp.dot(normed, piece, preferred_element_type=jnp.float32), approximate=False
    ).astype(jnp.bfloat16)


def contract(hidden, piece):
    return lax.dot_general(
        hidden, piece, (((1,), (1,)), ((), ())), preferred_element_type=jnp.float32
    )


HALVING_BITS = (0, 1, 3, 4, 2, 5, 7, 6)


def halving_order(rows):
    count, width = rows.shape
    nbits = len(HALVING_BITS)
    split = rows.reshape((count,) + (2,) * nbits + (width >> nbits,))
    order = (0,) + tuple(nbits - bit for bit in HALVING_BITS) + (nbits + 1,)
    return split.transpose(order).reshape(count, width)


def halving_sum(part, axes):
    size = 1
    for axis in axes:
        size *= lax.axis_size(axis)
    me = lax.axis_index(axes)
    for bit in HALVING_BITS:
        mine = (me >> bit) & 1
        halves = part.reshape((2, part.shape[0] // 2) + part.shape[1:])
        keep = lax.dynamic_index_in_dim(halves, mine, 0, keepdims=False)
        send = lax.dynamic_index_in_dim(halves, 1 - mine, 0, keepdims=False)
        pairs = [(i, i ^ (1 << bit)) for i in range(size)]
        part = keep + lax.ppermute(send, axes, pairs)
    return part


def targets_of(labels, count):
    classes = jnp.arange(NCLS, dtype=jnp.int32)
    onehot = (labels.reshape(count, 1) == classes[None, :]).astype(jnp.float32)
    return (onehot - 1.0 / NCLS).astype(jnp.bfloat16)


def on_device(features, dw_kernel, ln_gain, w_in, w_down, gamma, labels, valid):
    tiles, high, wide, width = features.shape
    tile = (width // LANES, LANES)
    padded = with_halo(features, (("row", 1), ("col", 2)), 3).astype(jnp.float32)
    padded = padded.reshape(padded.shape[:3] + tile)
    kernel = dw_kernel.astype(jnp.float32).reshape((KSIZE, KSIZE) + tile)
    conv = jnp.zeros((tiles, high, wide) + tile, jnp.float32)
    for i in range(KSIZE):
        for j in range(KSIZE):
            conv = conv + padded[:, i : i + high, j : j + wide] * kernel[i, j]
    count = tiles * high * wide
    normed = apply_norm(conv.reshape(count, *tile), ln_gain.reshape(tile)).reshape(count, width)
    hidden = expand(normed, lax.all_gather(w_in, "col", axis=1, tiled=True))
    branch = contract(hidden, lax.all_gather(w_down, "col", axis=1, tiled=True))
    out = (features.reshape(count, width).astype(jnp.float32) + gamma * branch).astype(jnp.bfloat16)
    keep = valid.reshape(count, 1)
    masked = out * keep.astype(jnp.bfloat16)
    both = lax.dot_general(
        halving_order(masked),
        jnp.concatenate([out, targets_of(labels, count)], axis=1),
        (((0,), (0,)), ((), ())),
        preferred_element_type=jnp.float32,
    )
    summed = halving_sum(both, ("row", "col"))
    gram_sum, cross_sum = summed[:, :width], summed[:, width:]
    total = float(tiles * high * lax.axis_size("row") * wide * lax.axis_size("col"))
    return (gram_sum / total, cross_sum / jnp.sqrt(jnp.float32(total)))


def solution(mesh):
    return jax.shard_map(
        on_device,
        mesh=mesh,
        in_specs=(
            P(None, "row", "col", None),
            P(),
            P(),
            P(None, "col"),
            P(None, "col"),
            P(),
            P(None, "row", "col"),
            P(None, "row", "col"),
        ),
        out_specs=(P(("row", "col"), None), P(("row", "col"), None)),
        check_vma=False,
    )
```

```python
import jax
import jax.numpy as jnp
from jax import lax
from jax.sharding import PartitionSpec as P

NCLS = 16
KSIZE = 7
LANES = 128


def with_halo(shard, sides, width):
    for axis, dim in sides:
        size, length = (lax.axis_size(axis), shard.shape[dim])
        up = [(i, (i + 1) % size) for i in range(size - 1)]
        down = [(j, i) for i, j in up]
        last = lax.slice_in_dim(shard, length - width, length, axis=dim)
        leading = lax.slice_in_dim(shard, 0, width, axis=dim)
        before = lax.ppermute(last, axis, up)
        after = lax.ppermute(leading, axis, down)
        shard = jnp.concatenate([before, shard, after], axis=dim)
    return shard


def apply_norm(rows, ln_gain):
    mean = jnp.mean(rows, axis=(-2, -1), keepdims=True)
    centered = rows - mean
    var = jnp.mean(centered * centered, axis=(-2, -1), keepdims=True)
    return (centered * lax.rsqrt(var + 1e-06) * ln_gain).astype(jnp.bfloat16)


def expand(normed, piece):
    return jax.nn.gelu(
        jnp.dot(normed, piece, preferred_element_type=jnp.float32), approximate=False
    ).astype(jnp.bfloat16)


def contract(hidden, piece):
    return lax.dot_general(
        hidden, piece, (((1,), (1,)), ((), ())), preferred_element_type=jnp.float32
    )


HALVING_BITS = ((0, 1, 3, 4, 2, 5, 7, 6), (0, 3, 1, 2, 4, 7, 5, 6))


def halving_order(rows):
    count, width = rows.shape
    nbits = len(HALVING_BITS[0])
    split = rows.reshape((count,) + (2,) * nbits + (width >> nbits,))
    halves = []
    for core, bits in enumerate(HALVING_BITS):
        half = lax.index_in_dim(split, core, nbits, keepdims=False)
        order = (0,) + tuple(nbits - bit for bit in bits[1:]) + (nbits,)
        halves.append(half.transpose(order).reshape(count, width // 2))
    return jnp.concatenate(halves, axis=1)


def halving_sum(part, axes):
    size = 1
    for axis in axes:
        size *= lax.axis_size(axis)
    me = lax.axis_index(axes)
    for step in range(len(HALVING_BITS[0])):
        bit = jnp.where(me & 1, HALVING_BITS[1][step], HALVING_BITS[0][step])
        mine = (me >> bit) & 1
        halves = part.reshape((2, part.shape[0] // 2) + part.shape[1:])
        keep = lax.dynamic_index_in_dim(halves, mine, 0, keepdims=False)
        send = lax.dynamic_index_in_dim(halves, 1 - mine, 0, keepdims=False)
        pairs = [(i, i ^ (1 << HALVING_BITS[i & 1][step])) for i in range(size)]
        part = keep + lax.ppermute(send, axes, pairs)
    return part


def targets_of(labels, count):
    classes = jnp.arange(NCLS, dtype=jnp.int32)
    onehot = (labels.reshape(count, 1) == classes[None, :]).astype(jnp.float32)
    return (onehot - 1.0 / NCLS).astype(jnp.bfloat16)


def on_device(features, dw_kernel, ln_gain, w_in, w_down, gamma, labels, valid):
    tiles, high, wide, width = features.shape
    tile = (width // LANES, LANES)
    padded = with_halo(features, (("row", 1), ("col", 2)), 3).astype(jnp.float32)
    padded = padded.reshape(padded.shape[:3] + tile)
    kernel = dw_kernel.astype(jnp.float32).reshape((KSIZE, KSIZE) + tile)
    conv = jnp.zeros((tiles, high, wide) + tile, jnp.float32)
    for i in range(KSIZE):
        for j in range(KSIZE):
            conv = conv + padded[:, i : i + high, j : j + wide] * kernel[i, j]
    count = tiles * high * wide
    normed = apply_norm(conv.reshape(count, *tile), ln_gain.reshape(tile)).reshape(count, width)
    hidden = expand(normed, lax.all_gather(w_in, "col", axis=1, tiled=True))
    branch = contract(hidden, lax.all_gather(w_down, "col", axis=1, tiled=True))
    out = (features.reshape(count, width).astype(jnp.float32) + gamma * branch).astype(jnp.bfloat16)
    keep = valid.reshape(count, 1)
    masked = out * keep.astype(jnp.bfloat16)
    both = lax.dot_general(
        halving_order(masked),
        jnp.concatenate([out, targets_of(labels, count)], axis=1),
        (((0,), (0,)), ((), ())),
        preferred_element_type=jnp.float32,
    )
    summed = halving_sum(both, ("row", "col"))
    gram_sum, cross_sum = summed[:, :width], summed[:, width:]
    total = float(tiles * high * lax.axis_size("row") * wide * lax.axis_size("col"))
    return (gram_sum / total, cross_sum / jnp.sqrt(jnp.float32(total)))


def solution(mesh):
    return jax.shard_map(
        on_device,
        mesh=mesh,
        in_specs=(
            P(None, "row", "col", None),
            P(),
            P(),
            P(None, "col"),
            P(None, "col"),
            P(),
            P(None, "row", "col"),
            P(None, "row", "col"),
        ),
        out_specs=(P(("row", "col"), None), P(("row", "col"), None)),
        check_vma=False,
    )
```

```python
import jax
import jax.numpy as jnp
from jax import lax
from jax.sharding import PartitionSpec as P

NCLS = 16
KSIZE = 7
LANES = 128


def with_halo(shard, sides, width):
    for axis, dim in sides:
        size, length = (lax.axis_size(axis), shard.shape[dim])
        up = [(i, (i + 1) % size) for i in range(size - 1)]
        down = [(j, i) for i, j in up]
        last = lax.slice_in_dim(shard, length - width, length, axis=dim)
        leading = lax.slice_in_dim(shard, 0, width, axis=dim)
        before = lax.ppermute(last, axis, up)
        after = lax.ppermute(leading, axis, down)
        shard = jnp.concatenate([before, shard, after], axis=dim)
    return shard


def apply_norm(rows, ln_gain):
    mean = jnp.mean(rows, axis=(-2, -1), keepdims=True)
    centered = rows - mean
    var = jnp.mean(centered * centered, axis=(-2, -1), keepdims=True)
    return (centered * lax.rsqrt(var + 1e-06) * ln_gain).astype(jnp.bfloat16)


def expand(normed, piece):
    return jax.nn.gelu(
        jnp.dot(normed, piece, preferred_element_type=jnp.float32), approximate=False
    ).astype(jnp.bfloat16)


def contract(hidden, piece):
    return lax.dot_general(
        hidden, piece, (((1,), (1,)), ((), ())), preferred_element_type=jnp.float32
    )


HALVING_BITS = ((0, 1, 3, 4, 2, 5, 7, 6), (0, 3, 1, 2, 4, 7, 5, 6))


def halving_order(rows):
    count, width = rows.shape
    bits = HALVING_BITS[0]
    split = rows.reshape((count,) + (2,) * len(bits) + (width >> len(bits),))
    order = (0,) + tuple(len(bits) - bit for bit in bits) + (len(bits) + 1,)
    return split.transpose(order).reshape(count, width)


def halving_sum(part, axes):
    size = 1
    for axis in axes:
        size *= lax.axis_size(axis)
    me = lax.axis_index(axes)
    for step in range(len(HALVING_BITS[0])):
        if HALVING_BITS[0][step] != HALVING_BITS[1][step] and (
            HALVING_BITS[0][step] == HALVING_BITS[1][step + 1]
        ):
            quarters = part.reshape((2, 2, part.shape[0] // 4) + part.shape[1:])
            swapped = jnp.swapaxes(quarters, 0, 1)
            part = jnp.where(me & 1, swapped, quarters).reshape(part.shape)
        bit = jnp.where(me & 1, HALVING_BITS[1][step], HALVING_BITS[0][step])
        mine = (me >> bit) & 1
        halves = part.reshape((2, part.shape[0] // 2) + part.shape[1:])
        keep = lax.dynamic_index_in_dim(halves, mine, 0, keepdims=False)
        send = lax.dynamic_index_in_dim(halves, 1 - mine, 0, keepdims=False)
        pairs = [(i, i ^ (1 << HALVING_BITS[i & 1][step])) for i in range(size)]
        part = keep + lax.ppermute(send, axes, pairs)
    return part


def targets_of(labels, count):
    classes = jnp.arange(NCLS, dtype=jnp.int32)
    onehot = (labels.reshape(count, 1) == classes[None, :]).astype(jnp.float32)
    return (onehot - 1.0 / NCLS).astype(jnp.bfloat16)


def on_device(features, dw_kernel, ln_gain, w_in, w_down, gamma, labels, valid):
    tiles, high, wide, width = features.shape
    tile = (width // LANES, LANES)
    padded = with_halo(features, (("row", 1), ("col", 2)), 3).astype(jnp.float32)
    padded = padded.reshape(padded.shape[:3] + tile)
    kernel = dw_kernel.astype(jnp.float32).reshape((KSIZE, KSIZE) + tile)
    conv = jnp.zeros((tiles, high, wide) + tile, jnp.float32)
    for i in range(KSIZE):
        for j in range(KSIZE):
            conv = conv + padded[:, i : i + high, j : j + wide] * kernel[i, j]
    count = tiles * high * wide
    normed = apply_norm(conv.reshape(count, *tile), ln_gain.reshape(tile)).reshape(count, width)
    hidden = expand(normed, lax.all_gather(w_in, "col", axis=1, tiled=True))
    branch = contract(hidden, lax.all_gather(w_down, "col", axis=1, tiled=True))
    out = (features.reshape(count, width).astype(jnp.float32) + gamma * branch).astype(jnp.bfloat16)
    keep = valid.reshape(count, 1)
    masked = out * keep.astype(jnp.bfloat16)
    both = lax.dot_general(
        halving_order(masked),
        jnp.concatenate([out, targets_of(labels, count)], axis=1),
        (((0,), (0,)), ((), ())),
        preferred_element_type=jnp.float32,
    )
    summed = halving_sum(both, ("row", "col"))
    gram_sum, cross_sum = summed[:, :width], summed[:, width:]
    total = float(tiles * high * lax.axis_size("row") * wide * lax.axis_size("col"))
    return (gram_sum / total, cross_sum / jnp.sqrt(jnp.float32(total)))


def solution(mesh):
    return jax.shard_map(
        on_device,
        mesh=mesh,
        in_specs=(
            P(None, "row", "col", None),
            P(),
            P(),
            P(None, "col"),
            P(None, "col"),
            P(),
            P(None, "row", "col"),
            P(None, "row", "col"),
        ),
        out_specs=(P(("row", "col"), None), P(("row", "col"), None)),
        check_vma=False,
    )
```

```python
import jax
import jax.numpy as jnp
from jax import lax
from jax.sharding import PartitionSpec as P

NCLS = 16
KSIZE = 7
LANES = 128


def with_halo(shard, sides, width):
    for axis, dim in sides:
        size, length = (lax.axis_size(axis), shard.shape[dim])
        up = [(i, (i + 1) % size) for i in range(size - 1)]
        down = [(j, i) for i, j in up]
        last = lax.slice_in_dim(shard, length - width, length, axis=dim)
        leading = lax.slice_in_dim(shard, 0, width, axis=dim)
        before = lax.ppermute(last, axis, up)
        after = lax.ppermute(leading, axis, down)
        shard = jnp.concatenate([before, shard, after], axis=dim)
    return shard


def apply_norm(rows, ln_gain):
    mean = jnp.mean(rows, axis=(-2, -1), keepdims=True)
    centered = rows - mean
    var = jnp.mean(centered * centered, axis=(-2, -1), keepdims=True)
    return (centered * lax.rsqrt(var + 1e-06) * ln_gain).astype(jnp.bfloat16)


def expand(normed, piece):
    return jax.nn.gelu(
        jnp.dot(normed, piece, preferred_element_type=jnp.float32), approximate=False
    ).astype(jnp.bfloat16)


def contract(hidden, piece):
    return lax.dot_general(
        hidden, piece, (((1,), (1,)), ((), ())), preferred_element_type=jnp.float32
    )


HALVING_BITS = ((0, 1, 3, 4, 2, 5, 7, 6), (0, 3, 1, 2, 4, 7, 5, 6))


def halving_order(rows):
    count, width = rows.shape
    bits = HALVING_BITS[0]
    split = rows.reshape((count,) + (2,) * len(bits) + (width >> len(bits),))
    order = (0,) + tuple(len(bits) - bit for bit in bits) + (len(bits) + 1,)
    return split.transpose(order).reshape(count, width)


def halving_sum(part, axes):
    size = 1
    for axis in axes:
        size *= lax.axis_size(axis)
    me = lax.axis_index(axes)
    core = me & 1
    for step in range(len(HALVING_BITS[0])):
        bit = jnp.where(core, HALVING_BITS[1][step], HALVING_BITS[0][step])
        mine = (me >> bit) & 1
        if HALVING_BITS[0][step] != HALVING_BITS[1][step] and (
            HALVING_BITS[0][step] == HALVING_BITS[1][step + 1]
        ):
            quarters = part.reshape((2, 2, part.shape[0] // 4) + part.shape[1:])
            rest = quarters.shape[2:]

            def half(value):
                pieces = []
                for other in (0, 1):
                    first = jnp.where(core, other, value)
                    second = jnp.where(core, value, other)
                    start = (first, second) + (0,) * len(rest)
                    piece = lax.dynamic_slice(quarters, start, (1, 1) + rest)
                    pieces.append(piece.reshape(rest))
                return jnp.concatenate(pieces, axis=0)

            keep, send = half(mine), half(1 - mine)
        else:
            halves = part.reshape((2, part.shape[0] // 2) + part.shape[1:])
            keep = lax.dynamic_index_in_dim(halves, mine, 0, keepdims=False)
            send = lax.dynamic_index_in_dim(halves, 1 - mine, 0, keepdims=False)
        pairs = [(i, i ^ (1 << HALVING_BITS[i & 1][step])) for i in range(size)]
        part = keep + lax.ppermute(send, axes, pairs)
    return part


def targets_of(labels, count):
    classes = jnp.arange(NCLS, dtype=jnp.int32)
    onehot = (labels.reshape(count, 1) == classes[None, :]).astype(jnp.float32)
    return (onehot - 1.0 / NCLS).astype(jnp.bfloat16)


def on_device(features, dw_kernel, ln_gain, w_in, w_down, gamma, labels, valid):
    tiles, high, wide, width = features.shape
    tile = (width // LANES, LANES)
    padded = with_halo(features, (("row", 1), ("col", 2)), 3).astype(jnp.float32)
    padded = padded.reshape(padded.shape[:3] + tile)
    kernel = dw_kernel.astype(jnp.float32).reshape((KSIZE, KSIZE) + tile)
    conv = jnp.zeros((tiles, high, wide) + tile, jnp.float32)
    for i in range(KSIZE):
        for j in range(KSIZE):
            conv = conv + padded[:, i : i + high, j : j + wide] * kernel[i, j]
    count = tiles * high * wide
    normed = apply_norm(conv.reshape(count, *tile), ln_gain.reshape(tile)).reshape(count, width)
    hidden = expand(normed, lax.all_gather(w_in, "col", axis=1, tiled=True))
    branch = contract(hidden, lax.all_gather(w_down, "col", axis=1, tiled=True))
    out = (features.reshape(count, width).astype(jnp.float32) + gamma * branch).astype(jnp.bfloat16)
    keep = valid.reshape(count, 1)
    masked = out * keep.astype(jnp.bfloat16)
    both = lax.dot_general(
        halving_order(masked),
        jnp.concatenate([out, targets_of(labels, count)], axis=1),
        (((0,), (0,)), ((), ())),
        preferred_element_type=jnp.float32,
    )
    summed = halving_sum(both, ("row", "col"))
    gram_sum, cross_sum = summed[:, :width], summed[:, width:]
    total = float(tiles * high * lax.axis_size("row") * wide * lax.axis_size("col"))
    return (gram_sum / total, cross_sum / jnp.sqrt(jnp.float32(total)))


def solution(mesh):
    return jax.shard_map(
        on_device,
        mesh=mesh,
        in_specs=(
            P(None, "row", "col", None),
            P(),
            P(),
            P(None, "col"),
            P(None, "col"),
            P(),
            P(None, "row", "col"),
            P(None, "row", "col"),
        ),
        out_specs=(P(("row", "col"), None), P(("row", "col"), None)),
        check_vma=False,
    )
```

```python
import jax
import jax.numpy as jnp
from jax import lax
from jax.sharding import PartitionSpec as P

NCLS = 16
KSIZE = 7
LANES = 128


def with_halo(shard, sides, width):
    for axis, dim in sides:
        size, length = (lax.axis_size(axis), shard.shape[dim])
        up = [(i, (i + 1) % size) for i in range(size - 1)]
        down = [(j, i) for i, j in up]
        last = lax.slice_in_dim(shard, length - width, length, axis=dim)
        leading = lax.slice_in_dim(shard, 0, width, axis=dim)
        before = lax.ppermute(last, axis, up)
        after = lax.ppermute(leading, axis, down)
        shard = jnp.concatenate([before, shard, after], axis=dim)
    return shard


def apply_norm(rows, ln_gain):
    mean = jnp.mean(rows, axis=(-2, -1), keepdims=True)
    centered = rows - mean
    var = jnp.mean(centered * centered, axis=(-2, -1), keepdims=True)
    return (centered * lax.rsqrt(var + 1e-06) * ln_gain).astype(jnp.bfloat16)


def expand(normed, piece):
    return jax.nn.gelu(
        jnp.dot(normed, piece, preferred_element_type=jnp.float32), approximate=False
    ).astype(jnp.bfloat16)


def contract(hidden, piece):
    return lax.dot_general(
        hidden, piece, (((1,), (1,)), ((), ())), preferred_element_type=jnp.float32
    )


HALVING_BITS = ((0, 1, 3, 4, 2, 5, 7, 6), (0, 3, 1, 2, 4, 7, 5, 6))


def halving_order(rows):
    count, width = rows.shape
    bits = HALVING_BITS[0]
    split = rows.reshape((count,) + (2,) * len(bits) + (width >> len(bits),))
    order = (0,) + tuple(len(bits) - bit for bit in bits) + (len(bits) + 1,)
    return split.transpose(order).reshape(count, width)


def halving_sum(part, axes, first):
    size = 1
    for axis in axes:
        size *= lax.axis_size(axis)
    me = lax.axis_index(axes)
    core = me & 1
    for step in range(first, len(HALVING_BITS[0])):
        bit = jnp.where(core, HALVING_BITS[1][step], HALVING_BITS[0][step])
        mine = (me >> bit) & 1
        if HALVING_BITS[0][step] != HALVING_BITS[1][step] and (
            HALVING_BITS[0][step] == HALVING_BITS[1][step + 1]
        ):
            quarters = part.reshape((2, 2, part.shape[0] // 4) + part.shape[1:])
            rest = quarters.shape[2:]

            def half(value):
                pieces = []
                for other in (0, 1):
                    first = jnp.where(core, other, value)
                    second = jnp.where(core, value, other)
                    start = (first, second) + (0,) * len(rest)
                    piece = lax.dynamic_slice(quarters, start, (1, 1) + rest)
                    pieces.append(piece.reshape(rest))
                return jnp.concatenate(pieces, axis=0)

            keep, send = half(mine), half(1 - mine)
        else:
            halves = part.reshape((2, part.shape[0] // 2) + part.shape[1:])
            keep = lax.dynamic_index_in_dim(halves, mine, 0, keepdims=False)
            send = lax.dynamic_index_in_dim(halves, 1 - mine, 0, keepdims=False)
        pairs = [(i, i ^ (1 << HALVING_BITS[i & 1][step])) for i in range(size)]
        part = keep + lax.ppermute(send, axes, pairs)
    return part


def targets_of(labels, count):
    classes = jnp.arange(NCLS, dtype=jnp.int32)
    onehot = (labels.reshape(count, 1) == classes[None, :]).astype(jnp.float32)
    return (onehot - 1.0 / NCLS).astype(jnp.bfloat16)


def on_device(features, dw_kernel, ln_gain, w_in, w_down, gamma, labels, valid):
    tiles, high, wide, width = features.shape
    tile = (width // LANES, LANES)
    padded = with_halo(features, (("row", 1), ("col", 2)), 3).astype(jnp.float32)
    padded = padded.reshape(padded.shape[:3] + tile)
    kernel = dw_kernel.astype(jnp.float32).reshape((KSIZE, KSIZE) + tile)
    conv = jnp.zeros((tiles, high, wide) + tile, jnp.float32)
    for i in range(KSIZE):
        for j in range(KSIZE):
            conv = conv + padded[:, i : i + high, j : j + wide] * kernel[i, j]
    count = tiles * high * wide
    normed = apply_norm(conv.reshape(count, *tile), ln_gain.reshape(tile)).reshape(count, width)
    hidden = expand(normed, lax.all_gather(w_in, "col", axis=1, tiled=True))
    axes = ("row", "col")
    size = lax.axis_size("row") * lax.axis_size("col")
    core = lax.axis_index(axes) & 1
    partner = [(i, i ^ 1) for i in range(size)]
    w_down_all = lax.all_gather(w_down, "col", axis=1, tiled=True)
    rows = features.reshape(count, width)
    keep = valid.reshape(count, 1).astype(jnp.bfloat16)
    targets = targets_of(labels, count) * keep
    mine, theirs = [], []
    for chunk in range(2):
        part = slice(chunk * count // 2, (chunk + 1) * count // 2)
        branch = contract(hidden[part], w_down_all)
        out = (rows[part].astype(jnp.float32) + gamma * branch).astype(jnp.bfloat16)
        both = jnp.concatenate([out, targets[part]], axis=1)
        mine.append(both)
        theirs.append(lax.ppermute(both, axes, partner))
    both = jnp.concatenate(mine + theirs, axis=0)
    kept = (both[:, width:width + 1] != 0).astype(jnp.bfloat16)
    masked = halving_order(both[:, :width] * kept)
    half = width // 2
    masked = lax.dynamic_slice_in_dim(masked, core * half, half, axis=1)
    summed = lax.dot_general(
        masked, both, (((0,), (0,)), ((), ())), preferred_element_type=jnp.float32
    )
    summed = halving_sum(summed, axes, 1)
    gram_sum, cross_sum = summed[:, :width], summed[:, width:]
    total = float(tiles * high * lax.axis_size("row") * wide * lax.axis_size("col"))
    return (gram_sum / total, cross_sum / jnp.sqrt(jnp.float32(total)))


def solution(mesh):
    return jax.shard_map(
        on_device,
        mesh=mesh,
        in_specs=(
            P(None, "row", "col", None),
            P(),
            P(),
            P(None, "col"),
            P(None, "col"),
            P(),
            P(None, "row", "col"),
            P(None, "row", "col"),
        ),
        out_specs=(P(("row", "col"), None), P(("row", "col"), None)),
        check_vma=False,
    )
```

```python
import jax
import jax.numpy as jnp
from jax import lax
from jax.sharding import PartitionSpec as P

NCLS = 16
KSIZE = 7
LANES = 128


def with_halo(shard, sides, width):
    for axis, dim in sides:
        size, length = (lax.axis_size(axis), shard.shape[dim])
        up = [(i, (i + 1) % size) for i in range(size - 1)]
        down = [(j, i) for i, j in up]
        last = lax.slice_in_dim(shard, length - width, length, axis=dim)
        leading = lax.slice_in_dim(shard, 0, width, axis=dim)
        before = lax.ppermute(last, axis, up)
        after = lax.ppermute(leading, axis, down)
        shard = jnp.concatenate([before, shard, after], axis=dim)
    return shard


def apply_norm(rows, ln_gain):
    mean = jnp.mean(rows, axis=(-2, -1), keepdims=True)
    centered = rows - mean
    var = jnp.mean(centered * centered, axis=(-2, -1), keepdims=True)
    return (centered * lax.rsqrt(var + 1e-06) * ln_gain).astype(jnp.bfloat16)


def expand(normed, piece):
    return jax.nn.gelu(
        jnp.dot(normed, piece, preferred_element_type=jnp.float32), approximate=False
    ).astype(jnp.bfloat16)


def contract(hidden, piece):
    return lax.dot_general(
        hidden, piece, (((1,), (1,)), ((), ())), preferred_element_type=jnp.float32
    )


HALVING_BITS = ((0, 1, 3, 4, 2, 5, 7, 6), (0, 3, 1, 2, 4, 7, 5, 6))


def halving_order(rows):
    count, width = rows.shape
    bits = HALVING_BITS[0]
    split = rows.reshape((count,) + (2,) * len(bits) + (width >> len(bits),))
    order = (0,) + tuple(len(bits) - bit for bit in bits) + (len(bits) + 1,)
    return split.transpose(order).reshape(count, width)


def halving_sum(part, axes, begin):
    size = 1
    for axis in axes:
        size *= lax.axis_size(axis)
    me = lax.axis_index(axes)
    core = me & 1
    for step in range(begin, len(HALVING_BITS[0])):
        bit = jnp.where(core, HALVING_BITS[1][step], HALVING_BITS[0][step])
        mine = (me >> bit) & 1
        if HALVING_BITS[0][step] != HALVING_BITS[1][step] and (
            HALVING_BITS[0][step] == HALVING_BITS[1][step + 1]
        ):
            quarters = part.reshape((2, 2, part.shape[0] // 4) + part.shape[1:])
            rest = quarters.shape[2:]

            def half(value):
                pieces = []
                for other in (0, 1):
                    first = jnp.where(core, other, value)
                    second = jnp.where(core, value, other)
                    start = (first, second) + (0,) * len(rest)
                    piece = lax.dynamic_slice(quarters, start, (1, 1) + rest)
                    pieces.append(piece.reshape(rest))
                return jnp.concatenate(pieces, axis=0)

            keep, send = half(mine), half(1 - mine)
        else:
            halves = part.reshape((2, part.shape[0] // 2) + part.shape[1:])
            keep = lax.dynamic_index_in_dim(halves, mine, 0, keepdims=False)
            send = lax.dynamic_index_in_dim(halves, 1 - mine, 0, keepdims=False)
        pairs = [(i, i ^ (1 << HALVING_BITS[i & 1][step])) for i in range(size)]
        part = keep + lax.ppermute(send, axes, pairs)
    return part


def targets_of(labels, count):
    classes = jnp.arange(NCLS, dtype=jnp.int32)
    onehot = (labels.reshape(count, 1) == classes[None, :]).astype(jnp.float32)
    return (onehot - 1.0 / NCLS).astype(jnp.bfloat16)


def on_device(features, dw_kernel, ln_gain, w_in, w_down, gamma, labels, valid):
    tiles, high, wide, width = features.shape
    tile = (width // LANES, LANES)
    padded = with_halo(features, (("row", 1), ("col", 2)), 3).astype(jnp.float32)
    padded = padded.reshape(padded.shape[:3] + tile)
    kernel = dw_kernel.astype(jnp.float32).reshape((KSIZE, KSIZE) + tile)
    conv = jnp.zeros((tiles, high, wide) + tile, jnp.float32)
    for i in range(KSIZE):
        for j in range(KSIZE):
            conv = conv + padded[:, i : i + high, j : j + wide] * kernel[i, j]
    count = tiles * high * wide
    normed = apply_norm(conv.reshape(count, *tile), ln_gain.reshape(tile)).reshape(count, width)
    hidden = expand(normed, lax.all_gather(w_in, "col", axis=1, tiled=True))
    branch = contract(hidden, lax.all_gather(w_down, "col", axis=1, tiled=True))
    out = (features.reshape(count, width).astype(jnp.float32) + gamma * branch).astype(jnp.bfloat16)
    keep = valid.reshape(count, 1)
    masked = out * keep.astype(jnp.bfloat16)
    axes = ("row", "col")
    core = lax.axis_index(axes) & 1
    ordered = halving_order(masked)
    rhs = jnp.concatenate([out, targets_of(labels, count)], axis=1)
    half = width // 2

    def rows_of(which):
        lhs = lax.dynamic_slice_in_dim(ordered, which * half, half, axis=1)
        return lax.dot_general(
            lhs, rhs, (((0,), (0,)), ((), ())), preferred_element_type=jnp.float32
        )

    size = lax.axis_size("row") * lax.axis_size("col")
    sent = lax.ppermute(rows_of(1 - core), axes, [(i, i ^ 1) for i in range(size)])
    kept = lax.optimization_barrier(rows_of(core))
    summed = halving_sum(kept + sent, axes, 1)
    gram_sum, cross_sum = summed[:, :width], summed[:, width:]
    total = float(tiles * high * lax.axis_size("row") * wide * lax.axis_size("col"))
    return (gram_sum / total, cross_sum / jnp.sqrt(jnp.float32(total)))


def solution(mesh):
    return jax.shard_map(
        on_device,
        mesh=mesh,
        in_specs=(
            P(None, "row", "col", None),
            P(),
            P(),
            P(None, "col"),
            P(None, "col"),
            P(),
            P(None, "row", "col"),
            P(None, "row", "col"),
        ),
        out_specs=(P(("row", "col"), None), P(("row", "col"), None)),
        check_vma=False,
    )
```

```python
import jax
import numpy as np
import jax.numpy as jnp
from jax import lax
from jax.sharding import PartitionSpec as P

NCLS = 16
KSIZE = 7
LANES = 128


def with_halo(shard, sides, width):
    for axis, dim in sides:
        size, length = (lax.axis_size(axis), shard.shape[dim])
        up = [(i, (i + 1) % size) for i in range(size - 1)]
        down = [(j, i) for i, j in up]
        last = lax.slice_in_dim(shard, length - width, length, axis=dim)
        leading = lax.slice_in_dim(shard, 0, width, axis=dim)
        before = lax.ppermute(last, axis, up)
        after = lax.ppermute(leading, axis, down)
        shard = jnp.concatenate([before, shard, after], axis=dim)
    return shard


def apply_norm(rows, ln_gain):
    mean = jnp.mean(rows, axis=(-2, -1), keepdims=True)
    centered = rows - mean
    var = jnp.mean(centered * centered, axis=(-2, -1), keepdims=True)
    return (centered * lax.rsqrt(var + 1e-06) * ln_gain).astype(jnp.bfloat16)


def expand(normed, piece):
    pre = jnp.dot(normed, piece, preferred_element_type=jnp.float32)
    return (0.5 * pre * (1.0 + lax.erf(pre * np.float32(np.sqrt(0.5))))).astype(jnp.bfloat16)


def contract(hidden, piece):
    return lax.dot_general(
        hidden, piece, (((1,), (1,)), ((), ())), preferred_element_type=jnp.float32
    )


HALVING_BITS = ((0, 1, 3, 4, 2, 5, 7, 6), (0, 3, 1, 2, 4, 7, 5, 6))


def halving_order(rows):
    count, width = rows.shape
    bits = HALVING_BITS[0]
    split = rows.reshape((count,) + (2,) * len(bits) + (width >> len(bits),))
    order = (0,) + tuple(len(bits) - bit for bit in bits) + (len(bits) + 1,)
    return split.transpose(order).reshape(count, width)


def halving_sum(part, axes, begin):
    size = 1
    for axis in axes:
        size *= lax.axis_size(axis)
    me = lax.axis_index(axes)
    core = me & 1
    for step in range(begin, len(HALVING_BITS[0])):
        bit = jnp.where(core, HALVING_BITS[1][step], HALVING_BITS[0][step])
        mine = (me >> bit) & 1
        if HALVING_BITS[0][step] != HALVING_BITS[1][step] and (
            HALVING_BITS[0][step] == HALVING_BITS[1][step + 1]
        ):
            quarters = part.reshape((2, 2, part.shape[0] // 4) + part.shape[1:])
            rest = quarters.shape[2:]

            def half(value):
                pieces = []
                for other in (0, 1):
                    first = jnp.where(core, other, value)
                    second = jnp.where(core, value, other)
                    start = (first, second) + (0,) * len(rest)
                    piece = lax.dynamic_slice(quarters, start, (1, 1) + rest)
                    pieces.append(piece.reshape(rest))
                return jnp.concatenate(pieces, axis=0)

            keep, send = half(mine), half(1 - mine)
        else:
            halves = part.reshape((2, part.shape[0] // 2) + part.shape[1:])
            keep = lax.dynamic_index_in_dim(halves, mine, 0, keepdims=False)
            send = lax.dynamic_index_in_dim(halves, 1 - mine, 0, keepdims=False)
        pairs = [(i, i ^ (1 << HALVING_BITS[i & 1][step])) for i in range(size)]
        part = keep + lax.ppermute(send, axes, pairs)
    return part


def targets_of(labels, count):
    classes = jnp.arange(NCLS, dtype=jnp.int32)
    onehot = (labels.reshape(count, 1) == classes[None, :]).astype(jnp.float32)
    return (onehot - 1.0 / NCLS).astype(jnp.bfloat16)


def on_device(features, dw_kernel, ln_gain, w_in, w_down, gamma, labels, valid):
    tiles, high, wide, width = features.shape
    tile = (width // LANES, LANES)
    padded = with_halo(features, (("row", 1), ("col", 2)), 3).astype(jnp.float32)
    padded = padded.reshape(padded.shape[:3] + tile)
    kernel = dw_kernel.astype(jnp.float32).reshape((KSIZE, KSIZE) + tile)
    conv = jnp.zeros((tiles, high, wide) + tile, jnp.float32)
    for i in range(KSIZE):
        for j in range(KSIZE):
            conv = conv + padded[:, i : i + high, j : j + wide] * kernel[i, j]
    count = tiles * high * wide
    normed = apply_norm(conv.reshape(count, *tile), ln_gain.reshape(tile)).reshape(count, width)
    hidden = expand(normed, lax.all_gather(w_in, "col", axis=1, tiled=True))
    branch = contract(hidden, lax.all_gather(w_down, "col", axis=1, tiled=True))
    out = (features.reshape(count, width).astype(jnp.float32) + gamma * branch).astype(jnp.bfloat16)
    keep = valid.reshape(count, 1)
    masked = out * keep.astype(jnp.bfloat16)
    axes = ("row", "col")
    core = lax.axis_index(axes) & 1
    ordered = halving_order(masked)
    rhs = jnp.concatenate([out, targets_of(labels, count)], axis=1)
    half = width // 2

    def rows_of(which):
        lhs = lax.dynamic_slice_in_dim(ordered, which * half, half, axis=1)
        return lax.dot_general(
            lhs, rhs, (((0,), (0,)), ((), ())), preferred_element_type=jnp.float32
        )

    size = lax.axis_size("row") * lax.axis_size("col")
    sent = lax.ppermute(rows_of(1 - core), axes, [(i, i ^ 1) for i in range(size)])
    kept = lax.optimization_barrier(rows_of(core))
    summed = halving_sum(kept + sent, axes, 1)
    gram_sum, cross_sum = summed[:, :width], summed[:, width:]
    total = float(tiles * high * lax.axis_size("row") * wide * lax.axis_size("col"))
    return (gram_sum / total, cross_sum / jnp.sqrt(jnp.float32(total)))


def solution(mesh):
    return jax.shard_map(
        on_device,
        mesh=mesh,
        in_specs=(
            P(None, "row", "col", None),
            P(),
            P(),
            P(None, "col"),
            P(None, "col"),
            P(),
            P(None, "row", "col"),
            P(None, "row", "col"),
        ),
        out_specs=(P(("row", "col"), None), P(("row", "col"), None)),
        check_vma=False,
    )
```

```python
import jax
import numpy as np
import jax.numpy as jnp
from jax import lax
from jax.sharding import Mesh, PartitionSpec as P

NCLS = 16
KSIZE = 7
COL = ("chip", "core")
LANES = 128


def with_halo(shard, sides, width):
    for axis, dim in sides:
        size, length = (lax.axis_size(axis), shard.shape[dim])
        up = [(i, (i + 1) % size) for i in range(size - 1)]
        down = [(j, i) for i, j in up]
        last = lax.slice_in_dim(shard, length - width, length, axis=dim)
        leading = lax.slice_in_dim(shard, 0, width, axis=dim)
        before = lax.ppermute(last, axis, up)
        after = lax.ppermute(leading, axis, down)
        shard = jnp.concatenate([before, shard, after], axis=dim)
    return shard


def apply_norm(rows, ln_gain):
    mean = jnp.mean(rows, axis=(-2, -1), keepdims=True)
    centered = rows - mean
    var = jnp.mean(centered * centered, axis=(-2, -1), keepdims=True)
    return (centered * lax.rsqrt(var + 1e-06) * ln_gain).astype(jnp.bfloat16)


def expand(normed, piece):
    pre = jnp.dot(normed, piece, preferred_element_type=jnp.float32)
    return (0.5 * pre * (1.0 + lax.erf(pre * np.float32(np.sqrt(0.5))))).astype(jnp.bfloat16)


def contract(hidden, piece):
    return lax.dot_general(
        hidden, piece, (((1,), (1,)), ((), ())), preferred_element_type=jnp.float32
    )


HALVING_BITS = ((0, 1, 3, 4, 2, 5, 7, 6), (0, 3, 1, 2, 4, 7, 5, 6))


def halving_order(rows):
    count, width = rows.shape
    bits = HALVING_BITS[0]
    split = rows.reshape((count,) + (2,) * len(bits) + (width >> len(bits),))
    order = (0,) + tuple(len(bits) - bit for bit in bits) + (len(bits) + 1,)
    return split.transpose(order).reshape(count, width)


def halving_sum(part, axes, begin):
    size = 1
    for axis in axes:
        size *= lax.axis_size(axis)
    me = lax.axis_index(axes)
    core = me & 1
    for step in range(begin, len(HALVING_BITS[0])):
        bit = jnp.where(core, HALVING_BITS[1][step], HALVING_BITS[0][step])
        mine = (me >> bit) & 1
        if HALVING_BITS[0][step] != HALVING_BITS[1][step] and (
            HALVING_BITS[0][step] == HALVING_BITS[1][step + 1]
        ):
            quarters = part.reshape((2, 2, part.shape[0] // 4) + part.shape[1:])
            rest = quarters.shape[2:]

            def half(value):
                pieces = []
                for other in (0, 1):
                    first = jnp.where(core, other, value)
                    second = jnp.where(core, value, other)
                    start = (first, second) + (0,) * len(rest)
                    piece = lax.dynamic_slice(quarters, start, (1, 1) + rest)
                    pieces.append(piece.reshape(rest))
                return jnp.concatenate(pieces, axis=0)

            keep, send = half(mine), half(1 - mine)
        else:
            halves = part.reshape((2, part.shape[0] // 2) + part.shape[1:])
            keep = lax.dynamic_index_in_dim(halves, mine, 0, keepdims=False)
            send = lax.dynamic_index_in_dim(halves, 1 - mine, 0, keepdims=False)
        pairs = [(i, i ^ (1 << HALVING_BITS[i & 1][step])) for i in range(size)]
        part = keep + lax.ppermute(send, axes, pairs)
    return part


def targets_of(labels, count):
    classes = jnp.arange(NCLS, dtype=jnp.int32)
    onehot = (labels.reshape(count, 1) == classes[None, :]).astype(jnp.float32)
    return (onehot - 1.0 / NCLS).astype(jnp.bfloat16)


def gather_hidden(piece):
    across = lax.all_gather(piece, COL[0], axis=1, tiled=True)
    return lax.all_gather(across, COL[1], axis=1, tiled=True)


def on_device(features, dw_kernel, ln_gain, w_in, w_down, gamma, labels, valid):
    tiles, high, wide, width = features.shape
    tile = (width // LANES, LANES)
    padded = with_halo(features, (("row", 1), (COL, 2)), 3).astype(jnp.float32)
    padded = padded.reshape(padded.shape[:3] + tile)
    kernel = dw_kernel.astype(jnp.float32).reshape((KSIZE, KSIZE) + tile)
    conv = jnp.zeros((tiles, high, wide) + tile, jnp.float32)
    for i in range(KSIZE):
        for j in range(KSIZE):
            conv = conv + padded[:, i : i + high, j : j + wide] * kernel[i, j]
    count = tiles * high * wide
    normed = apply_norm(conv.reshape(count, *tile), ln_gain.reshape(tile)).reshape(count, width)
    hidden = expand(normed, gather_hidden(w_in))
    branch = contract(hidden, gather_hidden(w_down))
    out = (features.reshape(count, width).astype(jnp.float32) + gamma * branch).astype(jnp.bfloat16)
    keep = valid.reshape(count, 1)
    masked = out * keep.astype(jnp.bfloat16)
    axes = ("row",) + COL
    core = lax.axis_index(axes) & 1
    ordered = halving_order(masked)
    rhs = jnp.concatenate([out, targets_of(labels, count)], axis=1)
    half = width // 2

    def rows_of(which):
        lhs = lax.dynamic_slice_in_dim(ordered, which * half, half, axis=1)
        return lax.dot_general(
            lhs, rhs, (((0,), (0,)), ((), ())), preferred_element_type=jnp.float32
        )

    size = lax.axis_size("row") * lax.axis_size(COL)
    sent = lax.ppermute(rows_of(1 - core), axes, [(i, i ^ 1) for i in range(size)])
    kept = lax.optimization_barrier(rows_of(core))
    summed = halving_sum(kept + sent, axes, 1)
    gram_sum, cross_sum = summed[:, :width], summed[:, width:]
    total = float(tiles * high * lax.axis_size("row") * wide * lax.axis_size(COL))
    return (gram_sum / total, cross_sum / jnp.sqrt(jnp.float32(total)))


def solution(mesh):
    rows, cols = mesh.devices.shape
    fine = Mesh(mesh.devices.reshape(rows, cols // 2, 2), ("row",) + COL)
    return jax.shard_map(
        on_device,
        mesh=fine,
        in_specs=(
            P(None, "row", COL, None),
            P(),
            P(),
            P(None, COL),
            P(None, COL),
            P(),
            P(None, "row", COL),
            P(None, "row", COL),
        ),
        out_specs=(P(("row",) + COL, None), P(("row",) + COL, None)),
        check_vma=False,
    )
```

```python
import jax
import numpy as np
import jax.numpy as jnp
from jax import lax
from jax.sharding import PartitionSpec as P

NCLS = 16
KSIZE = 7
LANES = 128


def with_halo(shard, sides, width):
    for axis, dim in sides:
        size, length = (lax.axis_size(axis), shard.shape[dim])
        up = [(i, (i + 1) % size) for i in range(size - 1)]
        down = [(j, i) for i, j in up]
        last = lax.slice_in_dim(shard, length - width, length, axis=dim)
        leading = lax.slice_in_dim(shard, 0, width, axis=dim)
        before = lax.ppermute(last, axis, up)
        after = lax.ppermute(leading, axis, down)
        shard = jnp.concatenate([before, shard, after], axis=dim)
    return shard


def apply_norm(rows, ln_gain):
    mean = jnp.mean(rows, axis=(-2, -1), keepdims=True)
    centered = rows - mean
    var = jnp.mean(centered * centered, axis=(-2, -1), keepdims=True)
    return (centered * lax.rsqrt(var + 1e-06) * ln_gain).astype(jnp.bfloat16)


def expand(normed, piece):
    pre = jnp.dot(normed, piece, preferred_element_type=jnp.float32)
    return (0.5 * pre * (1.0 + lax.erf(pre * np.float32(np.sqrt(0.5))))).astype(jnp.bfloat16)


def contract(hidden, piece):
    return lax.dot_general(
        hidden, piece, (((1,), (1,)), ((), ())), preferred_element_type=jnp.float32
    )


HALVING_BITS = ((0, 1, 3, 4, 2, 5, 7, 6), (0, 3, 1, 2, 4, 7, 5, 6))


def halving_order(rows):
    count, width = rows.shape
    bits = HALVING_BITS[0]
    split = rows.reshape((count,) + (2,) * len(bits) + (width >> len(bits),))
    order = (0,) + tuple(len(bits) - bit for bit in bits) + (len(bits) + 1,)
    return split.transpose(order).reshape(count, width)


def halving_sum(part, axes, begin):
    size = 1
    for axis in axes:
        size *= lax.axis_size(axis)
    me = lax.axis_index(axes)
    core = me & 1
    for step in range(begin, len(HALVING_BITS[0])):
        bit = jnp.where(core, HALVING_BITS[1][step], HALVING_BITS[0][step])
        mine = (me >> bit) & 1
        if HALVING_BITS[0][step] != HALVING_BITS[1][step] and (
            HALVING_BITS[0][step] == HALVING_BITS[1][step + 1]
        ):
            quarters = part.reshape((2, 2, part.shape[0] // 4) + part.shape[1:])
            rest = quarters.shape[2:]

            def half(value):
                pieces = []
                for other in (0, 1):
                    first = jnp.where(core, other, value)
                    second = jnp.where(core, value, other)
                    start = (first, second) + (0,) * len(rest)
                    piece = lax.dynamic_slice(quarters, start, (1, 1) + rest)
                    pieces.append(piece.reshape(rest))
                return jnp.concatenate(pieces, axis=0)

            keep, send = half(mine), half(1 - mine)
        else:
            halves = part.reshape((2, part.shape[0] // 2) + part.shape[1:])
            keep = lax.dynamic_index_in_dim(halves, mine, 0, keepdims=False)
            send = lax.dynamic_index_in_dim(halves, 1 - mine, 0, keepdims=False)
        pairs = [(i, i ^ (1 << HALVING_BITS[i & 1][step])) for i in range(size)]
        part = keep + lax.ppermute(send, axes, pairs)
    return part


def targets_of(labels, count):
    classes = jnp.arange(NCLS, dtype=jnp.int32)
    onehot = (labels.reshape(count, 1) == classes[None, :]).astype(jnp.float32)
    return (onehot - 1.0 / NCLS).astype(jnp.bfloat16)


def on_device(features, dw_kernel, ln_gain, w_in, w_down, gamma, labels, valid):
    tiles, high, wide, width = features.shape
    tile = (width // LANES, LANES)
    padded = with_halo(features, (("row", 1), ("col", 2)), 3).astype(jnp.float32)
    padded = padded.reshape(padded.shape[:3] + tile)
    kernel = dw_kernel.astype(jnp.float32).reshape((KSIZE, KSIZE) + tile)
    conv = jnp.zeros((tiles, high, wide) + tile, jnp.float32)
    for i in range(KSIZE):
        for j in range(KSIZE):
            conv = conv + padded[:, i : i + high, j : j + wide] * kernel[i, j]
    count = tiles * high * wide
    normed = apply_norm(conv.reshape(count, *tile), ln_gain.reshape(tile)).reshape(count, width)
    w_in_all, w_down_all = lax.all_gather(
        jnp.stack([w_in, w_down]), "col", axis=2, tiled=True
    )
    hidden = expand(normed, w_in_all)
    branch = contract(hidden, w_down_all)
    out = (features.reshape(count, width).astype(jnp.float32) + gamma * branch).astype(jnp.bfloat16)
    keep = valid.reshape(count, 1)
    masked = out * keep.astype(jnp.bfloat16)
    axes = ("row", "col")
    core = lax.axis_index(axes) & 1
    ordered = halving_order(masked)
    rhs = jnp.concatenate([out, targets_of(labels, count)], axis=1)
    half = width // 2

    def rows_of(which):
        lhs = lax.dynamic_slice_in_dim(ordered, which * half, half, axis=1)
        return lax.dot_general(
            lhs, rhs, (((0,), (0,)), ((), ())), preferred_element_type=jnp.float32
        )

    size = lax.axis_size("row") * lax.axis_size("col")
    sent = lax.ppermute(rows_of(1 - core), axes, [(i, i ^ 1) for i in range(size)])
    kept = lax.optimization_barrier(rows_of(core))
    summed = halving_sum(kept + sent, axes, 1)
    gram_sum, cross_sum = summed[:, :width], summed[:, width:]
    total = float(tiles * high * lax.axis_size("row") * wide * lax.axis_size("col"))
    return (gram_sum / total, cross_sum / jnp.sqrt(jnp.float32(total)))


def solution(mesh):
    return jax.shard_map(
        on_device,
        mesh=mesh,
        in_specs=(
            P(None, "row", "col", None),
            P(),
            P(),
            P(None, "col"),
            P(None, "col"),
            P(),
            P(None, "row", "col"),
            P(None, "row", "col"),
        ),
        out_specs=(P(("row", "col"), None), P(("row", "col"), None)),
        check_vma=False,
    )
```

```python
import jax
import numpy as np
import jax.numpy as jnp
from jax import lax
from jax.sharding import PartitionSpec as P

NCLS = 16
KSIZE = 7
LANES = 128


def with_halo(shard, sides, width):
    for axis, dim in sides:
        size, length = (lax.axis_size(axis), shard.shape[dim])
        up = [(i, (i + 1) % size) for i in range(size - 1)]
        down = [(j, i) for i, j in up]
        last = lax.slice_in_dim(shard, length - width, length, axis=dim)
        leading = lax.slice_in_dim(shard, 0, width, axis=dim)
        before = lax.ppermute(last, axis, up)
        after = lax.ppermute(leading, axis, down)
        shard = jnp.concatenate([before, shard, after], axis=dim)
    return shard


def apply_norm(rows, ln_gain):
    mean = jnp.mean(rows, axis=(-2, -1), keepdims=True)
    centered = rows - mean
    var = jnp.mean(centered * centered, axis=(-2, -1), keepdims=True)
    return (centered * lax.rsqrt(var + 1e-06) * ln_gain).astype(jnp.bfloat16)


def expand(normed, piece):
    pre = jnp.dot(normed, piece, preferred_element_type=jnp.float32)
    return (0.5 * pre * (1.0 + lax.erf(pre * np.float32(np.sqrt(0.5))))).astype(jnp.bfloat16)


def contract(hidden, piece):
    return lax.dot_general(
        hidden, piece, (((1,), (1,)), ((), ())), preferred_element_type=jnp.float32
    )


HALVING_BITS = ((0, 1, 3, 4, 2, 5, 7, 6), (0, 3, 1, 2, 4, 7, 5, 6))


def halving_order(rows):
    count, width = rows.shape
    bits = HALVING_BITS[0]
    split = rows.reshape((count,) + (2,) * len(bits) + (width >> len(bits),))
    order = (0,) + tuple(len(bits) - bit for bit in bits) + (len(bits) + 1,)
    return split.transpose(order).reshape(count, width)


def halving_sum(addends, axes, begin):
    size = 1
    for axis in axes:
        size *= lax.axis_size(axis)
    me = lax.axis_index(axes)
    core = me & 1
    for step in range(begin, len(HALVING_BITS[0])):
        bit = jnp.where(core, HALVING_BITS[1][step], HALVING_BITS[0][step])
        mine = (me >> bit) & 1
        keep, send = 0, 0
        for part in addends:
            if HALVING_BITS[0][step] != HALVING_BITS[1][step] and (
                HALVING_BITS[0][step] == HALVING_BITS[1][step + 1]
            ):
                quarters = part.reshape((2, 2, part.shape[0] // 4) + part.shape[1:])
                rest = quarters.shape[2:]

                def half(value):
                    pieces = []
                    for other in (0, 1):
                        first = jnp.where(core, other, value)
                        second = jnp.where(core, value, other)
                        start = (first, second) + (0,) * len(rest)
                        piece = lax.dynamic_slice(quarters, start, (1, 1) + rest)
                        pieces.append(piece.reshape(rest))
                    return jnp.concatenate(pieces, axis=0)

                keep, send = keep + half(mine), send + half(1 - mine)
            else:
                halves = part.reshape((2, part.shape[0] // 2) + part.shape[1:])
                keep = keep + lax.dynamic_index_in_dim(halves, mine, 0, keepdims=False)
                send = send + lax.dynamic_index_in_dim(halves, 1 - mine, 0, keepdims=False)
        pairs = [(i, i ^ (1 << HALVING_BITS[i & 1][step])) for i in range(size)]
        addends = [keep + lax.ppermute(send, axes, pairs)]
    return addends[0]


def targets_of(labels, count):
    classes = jnp.arange(NCLS, dtype=jnp.int32)
    onehot = (labels.reshape(count, 1) == classes[None, :]).astype(jnp.float32)
    return (onehot - 1.0 / NCLS).astype(jnp.bfloat16)


def on_device(features, dw_kernel, ln_gain, w_in, w_down, gamma, labels, valid):
    tiles, high, wide, width = features.shape
    tile = (width // LANES, LANES)
    padded = with_halo(features, (("row", 1), ("col", 2)), 3).astype(jnp.float32)
    padded = padded.reshape(padded.shape[:3] + tile)
    kernel = dw_kernel.astype(jnp.float32).reshape((KSIZE, KSIZE) + tile)
    conv = jnp.zeros((tiles, high, wide) + tile, jnp.float32)
    for i in range(KSIZE):
        for j in range(KSIZE):
            conv = conv + padded[:, i : i + high, j : j + wide] * kernel[i, j]
    count = tiles * high * wide
    normed = apply_norm(conv.reshape(count, *tile), ln_gain.reshape(tile)).reshape(count, width)
    w_in_all, w_down_all = lax.all_gather(
        jnp.stack([w_in, w_down]), "col", axis=2, tiled=True
    )
    hidden = expand(normed, w_in_all)
    branch = contract(hidden, w_down_all)
    out = (features.reshape(count, width).astype(jnp.float32) + gamma * branch).astype(jnp.bfloat16)
    keep = valid.reshape(count, 1)
    masked = out * keep.astype(jnp.bfloat16)
    axes = ("row", "col")
    core = lax.axis_index(axes) & 1
    ordered = halving_order(masked)
    rhs = jnp.concatenate([out, targets_of(labels, count)], axis=1)
    half = width // 2

    def rows_of(which):
        lhs = lax.dynamic_slice_in_dim(ordered, which * half, half, axis=1)
        return lax.dot_general(
            lhs, rhs, (((0,), (0,)), ((), ())), preferred_element_type=jnp.float32
        )

    size = lax.axis_size("row") * lax.axis_size("col")
    sent = lax.ppermute(rows_of(1 - core), axes, [(i, i ^ 1) for i in range(size)])
    kept = lax.optimization_barrier(rows_of(core))
    summed = halving_sum([kept, sent], axes, 1)
    gram_sum, cross_sum = summed[:, :width], summed[:, width:]
    total = float(tiles * high * lax.axis_size("row") * wide * lax.axis_size("col"))
    return (gram_sum / total, cross_sum / jnp.sqrt(jnp.float32(total)))


def solution(mesh):
    return jax.shard_map(
        on_device,
        mesh=mesh,
        in_specs=(
            P(None, "row", "col", None),
            P(),
            P(),
            P(None, "col"),
            P(None, "col"),
            P(),
            P(None, "row", "col"),
            P(None, "row", "col"),
        ),
        out_specs=(P(("row", "col"), None), P(("row", "col"), None)),
        check_vma=False,
    )
```

```python
import jax
import numpy as np
import jax.numpy as jnp
from jax import lax
from jax.sharding import PartitionSpec as P

NCLS = 16
KSIZE = 7
LANES = 128


def with_halo(shard, sides, width):
    for axis, dim in sides:
        size, length = (lax.axis_size(axis), shard.shape[dim])
        up = [(i, (i + 1) % size) for i in range(size - 1)]
        down = [(j, i) for i, j in up]
        last = lax.slice_in_dim(shard, length - width, length, axis=dim)
        leading = lax.slice_in_dim(shard, 0, width, axis=dim)
        before = lax.ppermute(last, axis, up)
        after = lax.ppermute(leading, axis, down)
        shard = jnp.concatenate([before, shard, after], axis=dim)
    return shard


def apply_norm(rows, ln_gain):
    mean = jnp.mean(rows, axis=(-2, -1), keepdims=True)
    centered = rows - mean
    var = jnp.mean(centered * centered, axis=(-2, -1), keepdims=True)
    return (centered * lax.rsqrt(var + 1e-06) * ln_gain).astype(jnp.bfloat16)


def expand(normed, piece):
    pre = jnp.dot(normed, piece, preferred_element_type=jnp.float32)
    return (0.5 * pre * (1.0 + lax.erf(pre * np.float32(np.sqrt(0.5))))).astype(jnp.bfloat16)


def contract(hidden, piece):
    return lax.dot_general(
        hidden, piece, (((1,), (1,)), ((), ())), preferred_element_type=jnp.float32
    )


HALVING_BITS = ((0, 1, 3, 4, 2, 5, 7, 6), (0, 3, 1, 2, 4, 7, 5, 6))


def halving_order(rows):
    count, width = rows.shape
    bits = HALVING_BITS[0]
    split = rows.reshape((count,) + (2,) * len(bits) + (width >> len(bits),))
    order = (0,) + tuple(len(bits) - bit for bit in bits) + (len(bits) + 1,)
    return split.transpose(order).reshape(count, width)


def halving_sum(part, axes, begin):
    size = 1
    for axis in axes:
        size *= lax.axis_size(axis)
    me = lax.axis_index(axes)
    core = me & 1
    for step in range(begin, len(HALVING_BITS[0]) - 2):
        bit = jnp.where(core, HALVING_BITS[1][step], HALVING_BITS[0][step])
        mine = (me >> bit) & 1
        if HALVING_BITS[0][step] != HALVING_BITS[1][step] and (
            HALVING_BITS[0][step] == HALVING_BITS[1][step + 1]
        ):
            quarters = part.reshape((2, 2, part.shape[0] // 4) + part.shape[1:])
            rest = quarters.shape[2:]

            def half(value):
                pieces = []
                for other in (0, 1):
                    first = jnp.where(core, other, value)
                    second = jnp.where(core, value, other)
                    start = (first, second) + (0,) * len(rest)
                    piece = lax.dynamic_slice(quarters, start, (1, 1) + rest)
                    pieces.append(piece.reshape(rest))
                return jnp.concatenate(pieces, axis=0)

            keep, send = half(mine), half(1 - mine)
        else:
            halves = part.reshape((2, part.shape[0] // 2) + part.shape[1:])
            keep = lax.dynamic_index_in_dim(halves, mine, 0, keepdims=False)
            send = lax.dynamic_index_in_dim(halves, 1 - mine, 0, keepdims=False)
        pairs = [(i, i ^ (1 << HALVING_BITS[i & 1][step])) for i in range(size)]
        part = keep + lax.ppermute(send, axes, pairs)
    last, final = len(HALVING_BITS[0]) - 2, len(HALVING_BITS[0]) - 1
    quarters = part.reshape((2, 2, part.shape[0] // 4) + part.shape[1:])
    rest = quarters.shape[2:]
    upper = (me >> jnp.where(core, HALVING_BITS[1][last], HALVING_BITS[0][last])) & 1
    lower = (me >> jnp.where(core, HALVING_BITS[1][final], HALVING_BITS[0][final])) & 1

    def quarter(first, second):
        start = (first, second) + (0,) * len(rest)
        return lax.dynamic_slice(quarters, start, (1, 1) + rest).reshape(rest)

    total = quarter(upper, lower)
    for flip_upper, flip_lower in ((1, 0), (0, 1), (1, 1)):
        pairs = [
            (i, i ^ (flip_upper << HALVING_BITS[i & 1][last]) ^ (flip_lower << HALVING_BITS[i & 1][final]))
            for i in range(size)
        ]
        piece = quarter(upper ^ flip_upper, lower ^ flip_lower)
        total = total + lax.ppermute(piece, axes, pairs)
    return total


def targets_of(labels, count):
    classes = jnp.arange(NCLS, dtype=jnp.int32)
    onehot = (labels.reshape(count, 1) == classes[None, :]).astype(jnp.float32)
    return (onehot - 1.0 / NCLS).astype(jnp.bfloat16)


def on_device(features, dw_kernel, ln_gain, w_in, w_down, gamma, labels, valid):
    tiles, high, wide, width = features.shape
    tile = (width // LANES, LANES)
    padded = with_halo(features, (("row", 1), ("col", 2)), 3).astype(jnp.float32)
    padded = padded.reshape(padded.shape[:3] + tile)
    kernel = dw_kernel.astype(jnp.float32).reshape((KSIZE, KSIZE) + tile)
    conv = jnp.zeros((tiles, high, wide) + tile, jnp.float32)
    for i in range(KSIZE):
        for j in range(KSIZE):
            conv = conv + padded[:, i : i + high, j : j + wide] * kernel[i, j]
    count = tiles * high * wide
    normed = apply_norm(conv.reshape(count, *tile), ln_gain.reshape(tile)).reshape(count, width)
    w_in_all, w_down_all = lax.all_gather(
        jnp.stack([w_in, w_down]), "col", axis=2, tiled=True
    )
    hidden = expand(normed, w_in_all)
    branch = contract(hidden, w_down_all)
    out = (features.reshape(count, width).astype(jnp.float32) + gamma * branch).astype(jnp.bfloat16)
    keep = valid.reshape(count, 1)
    masked = out * keep.astype(jnp.bfloat16)
    axes = ("row", "col")
    core = lax.axis_index(axes) & 1
    ordered = halving_order(masked)
    rhs = jnp.concatenate([out, targets_of(labels, count)], axis=1)
    half = width // 2

    def rows_of(which):
        lhs = lax.dynamic_slice_in_dim(ordered, which * half, half, axis=1)
        return lax.dot_general(
            lhs, rhs, (((0,), (0,)), ((), ())), preferred_element_type=jnp.float32
        )

    size = lax.axis_size("row") * lax.axis_size("col")
    sent = lax.ppermute(rows_of(1 - core), axes, [(i, i ^ 1) for i in range(size)])
    kept = lax.optimization_barrier(rows_of(core))
    summed = halving_sum(kept + sent, axes, 1)
    gram_sum, cross_sum = summed[:, :width], summed[:, width:]
    total = float(tiles * high * lax.axis_size("row") * wide * lax.axis_size("col"))
    return (gram_sum / total, cross_sum / jnp.sqrt(jnp.float32(total)))


def solution(mesh):
    return jax.shard_map(
        on_device,
        mesh=mesh,
        in_specs=(
            P(None, "row", "col", None),
            P(),
            P(),
            P(None, "col"),
            P(None, "col"),
            P(),
            P(None, "row", "col"),
            P(None, "row", "col"),
        ),
        out_specs=(P(("row", "col"), None), P(("row", "col"), None)),
        check_vma=False,
    )
```

```python
import jax
import numpy as np
import jax.numpy as jnp
from jax import lax
from jax.sharding import PartitionSpec as P

NCLS = 16
KSIZE = 7
LANES = 128


def with_halo(shard, sides, width):
    for axis, dim in sides:
        size, length = (lax.axis_size(axis), shard.shape[dim])
        up = [(i, (i + 1) % size) for i in range(size - 1)]
        down = [(j, i) for i, j in up]
        last = lax.slice_in_dim(shard, length - width, length, axis=dim)
        leading = lax.slice_in_dim(shard, 0, width, axis=dim)
        before = lax.ppermute(last, axis, up)
        after = lax.ppermute(leading, axis, down)
        shard = jnp.concatenate([before, shard, after], axis=dim)
    return shard


def apply_norm(rows, ln_gain):
    mean = jnp.mean(rows, axis=(-2, -1), keepdims=True)
    centered = rows - mean
    var = jnp.mean(centered * centered, axis=(-2, -1), keepdims=True)
    return (centered * lax.rsqrt(var + 1e-06) * ln_gain).astype(jnp.bfloat16)


def expand(normed, piece):
    pre = jnp.dot(normed, piece, preferred_element_type=jnp.float32)
    return (0.5 * pre * (1.0 + lax.erf(pre * np.float32(np.sqrt(0.5))))).astype(jnp.bfloat16)


def contract(hidden, piece):
    return lax.dot_general(
        hidden, piece, (((1,), (1,)), ((), ())), preferred_element_type=jnp.float32
    )


HALVING_BITS = ((0, 1, 3, 4, 2, 5, 7, 6), (0, 3, 1, 2, 4, 7, 5, 6))


def halving_order(rows):
    count, width = rows.shape
    bits = HALVING_BITS[0]
    split = rows.reshape((count,) + (2,) * len(bits) + (width >> len(bits),))
    order = (0,) + tuple(len(bits) - bit for bit in bits) + (len(bits) + 1,)
    return split.transpose(order).reshape(count, width)


def halving_sum(part, axes, steps):
    size = 1
    for axis in axes:
        size *= lax.axis_size(axis)
    me = lax.axis_index(axes)
    core = me & 1
    for step in steps:
        bit = jnp.where(core, HALVING_BITS[1][step], HALVING_BITS[0][step])
        mine = (me >> bit) & 1
        if HALVING_BITS[0][step] != HALVING_BITS[1][step] and (
            HALVING_BITS[0][step] == HALVING_BITS[1][step + 1]
        ):
            quarters = part.reshape((2, 2, part.shape[0] // 4) + part.shape[1:])
            rest = quarters.shape[2:]

            def half(value):
                pieces = []
                for other in (0, 1):
                    first = jnp.where(core, other, value)
                    second = jnp.where(core, value, other)
                    start = (first, second) + (0,) * len(rest)
                    piece = lax.dynamic_slice(quarters, start, (1, 1) + rest)
                    pieces.append(piece.reshape(rest))
                return jnp.concatenate(pieces, axis=0)

            keep, send = half(mine), half(1 - mine)
        else:
            halves = part.reshape((2, part.shape[0] // 2) + part.shape[1:])
            keep = lax.dynamic_index_in_dim(halves, mine, 0, keepdims=False)
            send = lax.dynamic_index_in_dim(halves, 1 - mine, 0, keepdims=False)
        pairs = [(i, i ^ (1 << HALVING_BITS[i & 1][step])) for i in range(size)]
        part = keep + lax.ppermute(send, axes, pairs)
    return part


def radix4(part, axes, upper_bits, lower_bits):
    size = 1
    for axis in axes:
        size *= lax.axis_size(axis)
    me = lax.axis_index(axes)
    core = me & 1
    quarters = part.reshape((2, 2, part.shape[0] // 4) + part.shape[1:])
    rest = quarters.shape[2:]
    upper = (me >> jnp.where(core, upper_bits[1], upper_bits[0])) & 1
    lower = (me >> jnp.where(core, lower_bits[1], lower_bits[0])) & 1

    def quarter(first, second):
        start = (first, second) + (0,) * len(rest)
        return lax.dynamic_slice(quarters, start, (1, 1) + rest).reshape(rest)

    total = quarter(upper, lower)
    for flip_upper, flip_lower in ((1, 0), (0, 1), (1, 1)):
        pairs = [
            (i, i ^ (flip_upper << upper_bits[i & 1]) ^ (flip_lower << lower_bits[i & 1]))
            for i in range(size)
        ]
        piece = quarter(upper ^ flip_upper, lower ^ flip_lower)
        total = total + lax.ppermute(piece, axes, pairs)
    return total


def targets_of(labels, count):
    classes = jnp.arange(NCLS, dtype=jnp.int32)
    onehot = (labels.reshape(count, 1) == classes[None, :]).astype(jnp.float32)
    return (onehot - 1.0 / NCLS).astype(jnp.bfloat16)


def on_device(features, dw_kernel, ln_gain, w_in, w_down, gamma, labels, valid):
    tiles, high, wide, width = features.shape
    tile = (width // LANES, LANES)
    padded = with_halo(features, (("row", 1), ("col", 2)), 3).astype(jnp.float32)
    padded = padded.reshape(padded.shape[:3] + tile)
    kernel = dw_kernel.astype(jnp.float32).reshape((KSIZE, KSIZE) + tile)
    conv = jnp.zeros((tiles, high, wide) + tile, jnp.float32)
    for i in range(KSIZE):
        for j in range(KSIZE):
            conv = conv + padded[:, i : i + high, j : j + wide] * kernel[i, j]
    count = tiles * high * wide
    normed = apply_norm(conv.reshape(count, *tile), ln_gain.reshape(tile)).reshape(count, width)
    w_in_all, w_down_all = lax.all_gather(
        jnp.stack([w_in, w_down]), "col", axis=2, tiled=True
    )
    hidden = expand(normed, w_in_all)
    branch = contract(hidden, w_down_all)
    out = (features.reshape(count, width).astype(jnp.float32) + gamma * branch).astype(jnp.bfloat16)
    keep = valid.reshape(count, 1)
    masked = out * keep.astype(jnp.bfloat16)
    axes = ("row", "col")
    core = lax.axis_index(axes) & 1
    ordered = halving_order(masked)
    rhs = jnp.concatenate([out, targets_of(labels, count)], axis=1)
    half = width // 2

    def rows_of(which):
        lhs = lax.dynamic_slice_in_dim(ordered, which * half, half, axis=1)
        return lax.dot_general(
            lhs, rhs, (((0,), (0,)), ((), ())), preferred_element_type=jnp.float32
        )

    size = lax.axis_size("row") * lax.axis_size("col")
    sent = lax.ppermute(rows_of(1 - core), axes, [(i, i ^ 1) for i in range(size)])
    kept = lax.optimization_barrier(rows_of(core))
    summed = halving_sum(kept + sent, axes, (1, 2))
    summed = radix4(summed, axes, (HALVING_BITS[0][3],) * 2, (HALVING_BITS[0][4],) * 2)
    summed = halving_sum(summed, axes, (5,))
    summed = radix4(summed, axes, tuple(b[6] for b in HALVING_BITS), tuple(b[7] for b in HALVING_BITS))
    gram_sum, cross_sum = summed[:, :width], summed[:, width:]
    total = float(tiles * high * lax.axis_size("row") * wide * lax.axis_size("col"))
    return (gram_sum / total, cross_sum / jnp.sqrt(jnp.float32(total)))


def solution(mesh):
    return jax.shard_map(
        on_device,
        mesh=mesh,
        in_specs=(
            P(None, "row", "col", None),
            P(),
            P(),
            P(None, "col"),
            P(None, "col"),
            P(),
            P(None, "row", "col"),
            P(None, "row", "col"),
        ),
        out_specs=(P(("row", "col"), None), P(("row", "col"), None)),
        check_vma=False,
    )
```

```python
import jax
import numpy as np
import jax.numpy as jnp
from jax import lax
from jax.sharding import PartitionSpec as P

NCLS = 16
KSIZE = 7
LANES = 128


def with_halo(shard, sides, width):
    for axis, dim in sides:
        size, length = (lax.axis_size(axis), shard.shape[dim])
        up = [(i, (i + 1) % size) for i in range(size - 1)]
        down = [(j, i) for i, j in up]
        last = lax.slice_in_dim(shard, length - width, length, axis=dim)
        leading = lax.slice_in_dim(shard, 0, width, axis=dim)
        before = lax.ppermute(last, axis, up)
        after = lax.ppermute(leading, axis, down)
        shard = jnp.concatenate([before, shard, after], axis=dim)
    return shard


def apply_norm(rows, ln_gain):
    mean = jnp.mean(rows, axis=(-2, -1), keepdims=True)
    centered = rows - mean
    var = jnp.mean(centered * centered, axis=(-2, -1), keepdims=True)
    return (centered * lax.rsqrt(var + 1e-06) * ln_gain).astype(jnp.bfloat16)


def expand(normed, piece):
    pre = jnp.dot(normed, piece, preferred_element_type=jnp.float32)
    return (0.5 * pre * (1.0 + lax.erf(pre * np.float32(np.sqrt(0.5))))).astype(jnp.bfloat16)


def contract(hidden, piece):
    return lax.dot_general(
        hidden, piece, (((1,), (1,)), ((), ())), preferred_element_type=jnp.float32
    )


HALVING_BITS = ((0, 1, 3, 4, 2, 5, 7, 6), (0, 3, 1, 2, 4, 7, 5, 6))


def halving_order(rows):
    count, width = rows.shape
    bits = HALVING_BITS[0]
    split = rows.reshape((count,) + (2,) * len(bits) + (width >> len(bits),))
    order = (0,) + tuple(len(bits) - bit for bit in bits) + (len(bits) + 1,)
    return split.transpose(order).reshape(count, width)


def halving_sum(part, axes, steps):
    size = 1
    for axis in axes:
        size *= lax.axis_size(axis)
    me = lax.axis_index(axes)
    core = me & 1
    for step in steps:
        bit = jnp.where(core, HALVING_BITS[1][step], HALVING_BITS[0][step])
        mine = (me >> bit) & 1
        if HALVING_BITS[0][step] != HALVING_BITS[1][step] and (
            HALVING_BITS[0][step] == HALVING_BITS[1][step + 1]
        ):
            quarters = part.reshape((2, 2, part.shape[0] // 4) + part.shape[1:])
            rest = quarters.shape[2:]

            def half(value):
                pieces = []
                for other in (0, 1):
                    first = jnp.where(core, other, value)
                    second = jnp.where(core, value, other)
                    start = (first, second) + (0,) * len(rest)
                    piece = lax.dynamic_slice(quarters, start, (1, 1) + rest)
                    pieces.append(piece.reshape(rest))
                return jnp.concatenate(pieces, axis=0)

            keep, send = half(mine), half(1 - mine)
        else:
            halves = part.reshape((2, part.shape[0] // 2) + part.shape[1:])
            keep = lax.dynamic_index_in_dim(halves, mine, 0, keepdims=False)
            send = lax.dynamic_index_in_dim(halves, 1 - mine, 0, keepdims=False)
        pairs = [(i, i ^ (1 << HALVING_BITS[i & 1][step])) for i in range(size)]
        part = keep + lax.ppermute(send, axes, pairs)
    return part


def radix4(part, axes, upper_bits, lower_bits):
    size = 1
    for axis in axes:
        size *= lax.axis_size(axis)
    me = lax.axis_index(axes)
    core = me & 1
    quarters = part.reshape((2, 2, part.shape[0] // 4) + part.shape[1:])
    rest = quarters.shape[2:]
    upper = (me >> jnp.where(core, upper_bits[1], upper_bits[0])) & 1
    lower = (me >> jnp.where(core, lower_bits[1], lower_bits[0])) & 1

    def quarter(first, second):
        start = (first, second) + (0,) * len(rest)
        return lax.dynamic_slice(quarters, start, (1, 1) + rest).reshape(rest)

    total = quarter(upper, lower)
    for flip_upper, flip_lower in ((1, 0), (0, 1), (1, 1)):
        pairs = [
            (i, i ^ (flip_upper << upper_bits[i & 1]) ^ (flip_lower << lower_bits[i & 1]))
            for i in range(size)
        ]
        piece = quarter(upper ^ flip_upper, lower ^ flip_lower)
        total = total + lax.ppermute(piece, axes, pairs)
    return total


def targets_of(labels, count):
    classes = jnp.arange(NCLS, dtype=jnp.int32)
    onehot = (labels.reshape(count, 1) == classes[None, :]).astype(jnp.float32)
    return (onehot - 1.0 / NCLS).astype(jnp.bfloat16)


def on_device(features, dw_kernel, ln_gain, w_in, w_down, gamma, labels, valid):
    tiles, high, wide, width = features.shape
    tile = (width // LANES, LANES)
    padded = with_halo(features, (("row", 1), ("col", 2)), 3).astype(jnp.float32)
    padded = padded.reshape(padded.shape[:3] + tile)
    kernel = dw_kernel.astype(jnp.float32).reshape((KSIZE, KSIZE) + tile)
    conv = jnp.zeros((tiles, high, wide) + tile, jnp.float32)
    for i in range(KSIZE):
        for j in range(KSIZE):
            conv = conv + padded[:, i : i + high, j : j + wide] * kernel[i, j]
    count = tiles * high * wide
    normed = apply_norm(conv.reshape(count, *tile), ln_gain.reshape(tile)).reshape(count, width)
    w_in_all, w_down_all = lax.all_gather(
        jnp.stack([w_in, w_down]), "col", axis=2, tiled=True
    )
    hidden = expand(normed, w_in_all)
    branch = contract(hidden, w_down_all)
    out = (features.reshape(count, width).astype(jnp.float32) + gamma * branch).astype(jnp.bfloat16)
    keep = valid.reshape(count, 1)
    masked = out * keep.astype(jnp.bfloat16)
    axes = ("row", "col")
    core = lax.axis_index(axes) & 1
    ordered = halving_order(masked)
    rhs = jnp.concatenate([out, targets_of(labels, count)], axis=1)
    half = width // 2

    def rows_of(which):
        lhs = lax.dynamic_slice_in_dim(ordered, which * half, half, axis=1)
        return lax.dot_general(
            lhs, rhs, (((0,), (0,)), ((), ())), preferred_element_type=jnp.float32
        )

    size = lax.axis_size("row") * lax.axis_size("col")
    sent = lax.ppermute(rows_of(1 - core), axes, [(i, i ^ 1) for i in range(size)])
    kept = lax.optimization_barrier(rows_of(core))
    summed = radix4(kept + sent, axes, (HALVING_BITS[0][1],) * 2, (HALVING_BITS[0][2],) * 2)
    summed = halving_sum(summed, axes, (3, 4, 5))
    summed = radix4(summed, axes, tuple(b[6] for b in HALVING_BITS), tuple(b[7] for b in HALVING_BITS))
    gram_sum, cross_sum = summed[:, :width], summed[:, width:]
    total = float(tiles * high * lax.axis_size("row") * wide * lax.axis_size("col"))
    return (gram_sum / total, cross_sum / jnp.sqrt(jnp.float32(total)))


def solution(mesh):
    return jax.shard_map(
        on_device,
        mesh=mesh,
        in_specs=(
            P(None, "row", "col", None),
            P(),
            P(),
            P(None, "col"),
            P(None, "col"),
            P(),
            P(None, "row", "col"),
            P(None, "row", "col"),
        ),
        out_specs=(P(("row", "col"), None), P(("row", "col"), None)),
        check_vma=False,
    )
```
